256 devices in a mesh: tp: 4 (over y_lo, core), pr: 64 (over z, y_hi, x).
Axes of the slice: x: 4, y: 4 (y_hi: 2, y_lo: 2; y = y_hi * 2 + y_lo), z: 8, core: 2. Of those that a mesh axis runs over, the one named last changes fastest.
Arguments:
- embed_table: bfloat16 [128256, 8192], P(('tp', 'pr')), may hold values from -13 to 13
- suffix_ids: int32 [20], replicated, may hold values from 0 to 128255
- context: bfloat16 [384, 44, 8192], P('pr', None, 'tp'), may hold values from -6 to 6
- prompt_len: int32 [384], P('pr'), may hold values from 8 to 32
- norm_gain: bfloat16 [8192], replicated, may hold values from 0.5 to 10
- w_query: bfloat16 [8192, 4096], P('pr', 'tp'), may hold values from -0.0625 to 0.0625
- key_projection_weight: bfloat16 [8192, 512], P('pr', 'tp'), may hold values from -0.0625 to 0.0625
- value_projection_weight: bfloat16 [8192, 512], P('pr', 'tp'), may hold values from -0.0625 to 0.0625
- ctx_grad: bfloat16 [384, 32, 4096], P('pr', None, 'tp'), may hold values from -6 to 6
Outputs:
- token_grads: float32 [20, 128256], P(None, ('tp', 'pr'))
The draws below stay inside these ranges and needn't reach their ends.
All inputs are finite; a program needn't handle non-finite values.
Results may differ from the reference program's by a relative error of at most 0.02.
The reference program's roundings to bfloat16 on the way count: a program that leaves them out, or rounds other values in their place, can miss the bound.
Values may be sent and summed in bfloat16 or wider, within the bound.
No kernel may reach another device: no remote copies, remote signals or barrier semaphores. Data moves between devices by JAX's collectives and lax.ppermute only.
A program may use at most 128 MiB of HBM per device.

```python
import jax
import jax.numpy as jnp
from jax import lax

MODEL_WIDTH = 8192
HEAD_SIZE = 128
VOCAB = 128256
QUERY_HEAD_COUNT = 32
KEY_VALUE_HEADS = 4
PLEN = 32
SUFFIX_TOKENS = 20
SEQUENCE_TOKENS = 64
CTX = 44
QUERY_ROW_COUNT = 32
PROMPTS = 384


def draw_embed_table(key, part):
    subkeys = jax.random.split(key, 3)
    row_frac = jnp.arange(VOCAB).astype(jnp.float32) / VOCAB
    row_noise = jax.random.uniform(subkeys[1], (VOCAB,), jnp.float32)
    col_log = jax.random.uniform(subkeys[2], (MODEL_WIDTH,), jnp.float32)
    base_draw = jnp.clip(jax.random.normal(subkeys[0], (VOCAB, MODEL_WIDTH), jnp.float32), -4.0, 4.0)
    row_log = 0.5 * row_frac + 0.5 * row_noise
    scale_rows = jnp.power(10.0, row_log)[:, None]
    scale_cols = jnp.power(10.0, col_log)[None, :]
    return (0.02 * base_draw * scale_rows * scale_cols).astype(jnp.bfloat16)


def draw_norm_gain(key, part):
    values = jax.random.uniform(key, (MODEL_WIDTH,), jnp.float32, 0.7, 1.3)
    return values.astype(jnp.bfloat16)


def with_ends(array, key, low, largest):
    extent = array.shape
    spot = [jax.random.randint(jax.random.fold_in(key, axis), (), 0, extent[axis]) for axis in range(len(extent))]
    array = array.at[tuple(spot)].set(low)
    longest = extent.index(max(extent))
    spot[longest] = (spot[longest] + 1) % extent[longest]
    return array.at[tuple(spot)].set(largest)


def steps_of(key, shape, shards, low, high):
    level, own = 1.0, jax.random.fold_in(key, 6)
    for position, blocks in shards:
        heights = jnp.exp(jax.random.uniform(jax.random.fold_in(own, position), (blocks,), jnp.float32, low / len(shards), high / len(shards)))
        level = level * jnp.repeat(heights, shape[position] // blocks).reshape([-1 if axis == position else 1 for axis in range(len(shape))])
    return level


def bell_draw(rng, shape, width, reach, cuts=(), held_as=jnp.bfloat16):
    level = steps_of(rng, shape, cuts, -0.22, 0.18) if cuts else 1.0
    array = jax.random.normal(rng, shape, jnp.float32) * width * level
    return jnp.minimum(jnp.maximum(array, -reach), reach).astype(held_as)


def setup_inputs(seed: int = 0) -> dict:
    keys = jax.random.split(jax.random.key(seed), 10)
    return {
        "embed_table": draw_embed_table(jax.random.fold_in(keys[9], 71), 0),
        "suffix_ids": with_ends(jax.random.randint(keys[1], (SUFFIX_TOKENS,), 0, VOCAB), jax.random.fold_in(keys[1], 1), 0, VOCAB - 1).astype(jnp.int32),
        "context": bell_draw(keys[2], (PROMPTS, CTX, MODEL_WIDTH), 1.0, 6.0, ((0, 64), (2, 4))),
        "prompt_len": with_ends(jax.random.randint(keys[3], (PROMPTS,), PLEN // 4, PLEN + 1), jax.random.fold_in(keys[3], 1), PLEN // 4, PLEN).astype(jnp.int32),
        "norm_gain": draw_norm_gain(jax.random.fold_in(keys[9], 71), 0),
        "w_query": bell_draw(keys[5], (MODEL_WIDTH, QUERY_HEAD_COUNT * HEAD_SIZE), MODEL_WIDTH ** -0.5, 0.0625, ((0, 64), (1, 4))),
        "key_projection_weight": bell_draw(keys[6], (MODEL_WIDTH, KEY_VALUE_HEADS * HEAD_SIZE), MODEL_WIDTH ** -0.5, 0.0625, ((0, 64), (1, 4))),
        "value_projection_weight": bell_draw(keys[7], (MODEL_WIDTH, KEY_VALUE_HEADS * HEAD_SIZE), MODEL_WIDTH ** -0.5, 0.0625, ((0, 64), (1, 4))),
        "ctx_grad": bell_draw(keys[8], (PROMPTS, QUERY_ROW_COUNT, QUERY_HEAD_COUNT * HEAD_SIZE), 1.0, 6.0, ((0, 64), (2, 4))),
    }


NORM_EPS = 1e-05
VOCAB_EPS = 1e-06
ROPE_BASE = 500000.0

def rope_tables(count):
    positions = jnp.arange(count).astype(jnp.float32)
    frequency = ROPE_BASE ** (-(jnp.arange(HEAD_SIZE // 2).astype(jnp.float32) * (2.0 / HEAD_SIZE)))
    angles = positions[:, None] * frequency[None, :]
    return (jnp.cos(angles), jnp.sin(angles))

def apply_rotation(tensor, cosine_table, sine_lookup_table, direction):
    half_width = tensor.shape[-1] // 2
    first_half = tensor[..., :half_width]
    second_half = tensor[..., half_width:]
    cos_wide = cosine_table[:, None, :]
    sin_wide = sine_lookup_table[:, None, :] * direction
    return jnp.concatenate([first_half * cos_wide - second_half * sin_wide, second_half * cos_wide + first_half * sin_wide], -1)

def normalize(tokens, norm_gain):
    tokens_f = tokens.astype(jnp.float32)
    inverse = lax.rsqrt(lax.optimization_barrier(jnp.mean(tokens_f * tokens_f, -1, keepdims=True)) + NORM_EPS)
    return (tokens_f * inverse * norm_gain.astype(jnp.float32)).astype(jnp.bfloat16)

def prompt_terms(context_row, length, gradient_row_block, suffix_rows, norm_gain, w_query, key_projection_weight, value_projection_weight):
    query_group_width = QUERY_HEAD_COUNT // KEY_VALUE_HEADS
    tokens = jnp.concatenate([context_row[:PLEN], suffix_rows, context_row[PLEN:]], 0)
    normed = normalize(tokens, norm_gain)
    query_matrix = jnp.dot(normed[PLEN:], w_query, preferred_element_type=jnp.float32)
    projected_key_rows = jnp.dot(normed, key_projection_weight, preferred_element_type=jnp.float32)
    projected_value_rows = jnp.dot(normed, value_projection_weight, preferred_element_type=jnp.float32)
    cosine_table, sine_lookup_table = rope_tables(SEQUENCE_TOKENS)
    query_matrix = apply_rotation(query_matrix.reshape(QUERY_ROW_COUNT, QUERY_HEAD_COUNT, HEAD_SIZE), cosine_table[PLEN:], sine_lookup_table[PLEN:], 1.0).astype(jnp.bfloat16)
    query_matrix = query_matrix.reshape(QUERY_ROW_COUNT, KEY_VALUE_HEADS, query_group_width, HEAD_SIZE)
    projected_key_rows = apply_rotation(projected_key_rows.reshape(SEQUENCE_TOKENS, KEY_VALUE_HEADS, HEAD_SIZE), cosine_table, sine_lookup_table, 1.0).astype(jnp.bfloat16)
    projected_value_rows = projected_value_rows.reshape(SEQUENCE_TOKENS, KEY_VALUE_HEADS, HEAD_SIZE).astype(jnp.bfloat16)
    context_gradient_rows = gradient_row_block.reshape(QUERY_ROW_COUNT, KEY_VALUE_HEADS, query_group_width, HEAD_SIZE)
    score_scale = HEAD_SIZE ** (-0.5)
    scores = jnp.einsum('ikgd,jkd->kgij', query_matrix.astype(jnp.float32), projected_key_rows.astype(jnp.float32)) * score_scale
    query_pos = PLEN + jnp.arange(QUERY_ROW_COUNT)
    key_pos = jnp.arange(SEQUENCE_TOKENS)
    visible = (key_pos[None, :] <= query_pos[:, None]) & (key_pos[None, :] >= PLEN - length)
    scores = jnp.where(visible, scores, -1e+30)
    row_max = lax.optimization_barrier(jnp.max(scores, -1, keepdims=True))
    expanded = jnp.where(visible, jnp.exp(scores - row_max), 0.0)
    attention = expanded / lax.optimization_barrier(jnp.sum(expanded, -1, keepdims=True))
    attention_low = attention.astype(jnp.bfloat16)
    prob_grads = jnp.einsum('ikgd,jkd->kgij', context_gradient_rows.astype(jnp.float32), projected_value_rows.astype(jnp.float32))
    row_dot = lax.optimization_barrier(jnp.sum(attention * prob_grads, -1, keepdims=True))
    score_grads = (attention * (prob_grads - row_dot) * score_scale).astype(jnp.bfloat16)
    query_gradient = jnp.einsum('kgij,jkd->ikgd', score_grads[:, :, :SUFFIX_TOKENS, :].astype(jnp.float32), projected_key_rows.astype(jnp.float32))
    key_gradient = jnp.einsum('kgij,ikgd->jkd', score_grads[..., PLEN:PLEN + SUFFIX_TOKENS].astype(jnp.float32), query_matrix.astype(jnp.float32))
    value_gradient = jnp.einsum('kgij,ikgd->jkd', attention_low[..., PLEN:PLEN + SUFFIX_TOKENS].astype(jnp.float32), context_gradient_rows.astype(jnp.float32))
    query_gradient = apply_rotation(query_gradient.reshape(SUFFIX_TOKENS, QUERY_HEAD_COUNT, HEAD_SIZE), cosine_table[PLEN:PLEN + SUFFIX_TOKENS], sine_lookup_table[PLEN:PLEN + SUFFIX_TOKENS], -1.0)
    key_gradient = apply_rotation(key_gradient, cosine_table[PLEN:PLEN + SUFFIX_TOKENS], sine_lookup_table[PLEN:PLEN + SUFFIX_TOKENS], -1.0)
    return (query_gradient.reshape(SUFFIX_TOKENS, QUERY_HEAD_COUNT * HEAD_SIZE), key_gradient.reshape(SUFFIX_TOKENS, KEY_VALUE_HEADS * HEAD_SIZE), value_gradient.reshape(SUFFIX_TOKENS, KEY_VALUE_HEADS * HEAD_SIZE))

def reference(embed_table, suffix_ids, context, prompt_len, norm_gain, w_query, key_projection_weight, value_projection_weight, ctx_grad):
    suffix_rows = jnp.take(embed_table, suffix_ids, axis=0)

    def scan_step(running, prompt_items):
        terms = prompt_terms(prompt_items[0], prompt_items[1], prompt_items[2], suffix_rows, norm_gain, w_query, key_projection_weight, value_projection_weight)
        return ((running[0] + terms[0], running[1] + terms[1], running[2] + terms[2]), None)
    starting_state = (jnp.zeros((SUFFIX_TOKENS, QUERY_HEAD_COUNT * HEAD_SIZE), jnp.float32), jnp.zeros((SUFFIX_TOKENS, KEY_VALUE_HEADS * HEAD_SIZE), jnp.float32), jnp.zeros((SUFFIX_TOKENS, KEY_VALUE_HEADS * HEAD_SIZE), jnp.float32))
    totals, _ = lax.scan(scan_step, starting_state, (context, prompt_len, ctx_grad))
    query_total = totals[0].astype(jnp.bfloat16)
    key_total = totals[1].astype(jnp.bfloat16)
    value_total = totals[2].astype(jnp.bfloat16)
    hidden_grad = jnp.dot(query_total, w_query.T, preferred_element_type=jnp.float32)
    hidden_grad = hidden_grad + jnp.dot(key_total, key_projection_weight.T, preferred_element_type=jnp.float32)
    hidden_grad = hidden_grad + jnp.dot(value_total, value_projection_weight.T, preferred_element_type=jnp.float32)
    suffix_f = suffix_rows.astype(jnp.float32)
    inverse = lax.rsqrt(lax.optimization_barrier(jnp.mean(suffix_f * suffix_f, -1, keepdims=True)) + NORM_EPS)
    scaled = norm_gain.astype(jnp.float32) * hidden_grad
    projection = lax.optimization_barrier(jnp.sum(scaled * suffix_f, -1, keepdims=True))
    input_grad = (scaled * inverse - suffix_f * projection * inverse ** 3 / MODEL_WIDTH).astype(jnp.bfloat16)
    token_scores = jnp.dot(input_grad, embed_table.T, preferred_element_type=jnp.float32)
    mean_square = lax.optimization_barrier(jnp.mean(token_scores * token_scores, -1, keepdims=True))
    return token_scores * lax.rsqrt(mean_square + VOCAB_EPS)
```

```python
import jax
import jax.numpy as jnp
from jax import lax
from jax.sharding import PartitionSpec as P

MODEL_WIDTH = 8192
HEAD_SIZE = 128
VOCAB = 128256
PLEN = 32
SUFFIX_TOKENS = 20
SEQUENCE_TOKENS = 64
QUERY_ROW_COUNT = 32


NORM_EPS = 1e-05
VOCAB_EPS = 1e-06
ROPE_BASE = 500000.0


def rope_tables(count):
    positions = jnp.arange(count).astype(jnp.float32)
    frequency = ROPE_BASE ** (-(jnp.arange(HEAD_SIZE // 2).astype(jnp.float32) * (2.0 / HEAD_SIZE)))
    angles = positions[:, None] * frequency[None, :]
    return (jnp.cos(angles), jnp.sin(angles))


def apply_rotation(tensor, cosine_table, sine_lookup_table, direction):
    half_width = tensor.shape[-1] // 2
    first_half = tensor[..., :half_width]
    second_half = tensor[..., half_width:]
    cos_wide = cosine_table[:, None, :]
    sin_wide = sine_lookup_table[:, None, :] * direction
    return jnp.concatenate(
        [
            first_half * cos_wide - second_half * sin_wide,
            second_half * cos_wide + first_half * sin_wide,
        ],
        -1,
    )


def normalize(tokens, norm_gain):
    tokens_f = tokens.astype(jnp.float32)
    inverse = lax.rsqrt(jnp.mean(tokens_f * tokens_f, -1, keepdims=True) + NORM_EPS)
    return (tokens_f * inverse * norm_gain.astype(jnp.float32)).astype(jnp.bfloat16)


def attention_grads(
    query_matrix, projected_key_rows, projected_value_rows, context_gradient_rows, lengths
):
    score_scale = HEAD_SIZE ** (-0.5)
    scores = (
        jnp.einsum(
            "pikgd,pjkd->pkgij",
            query_matrix,
            projected_key_rows,
            preferred_element_type=jnp.float32,
        )
        * score_scale
    )
    query_pos = PLEN + jnp.arange(QUERY_ROW_COUNT)
    key_pos = jnp.arange(SEQUENCE_TOKENS)
    causal = key_pos[None, :] <= query_pos[:, None]
    unpadded = key_pos[None, :] >= (PLEN - lengths)[:, None]
    visible = (causal[None, :, :] & unpadded[:, None, :])[:, None, None, :, :]
    scores = jnp.where(visible, scores, -1e30)
    row_max = jnp.max(scores, -1, keepdims=True)
    expanded = jnp.where(visible, jnp.exp(scores - row_max), 0.0)
    attention = expanded / jnp.sum(expanded, -1, keepdims=True)
    attention_low = attention.astype(jnp.bfloat16)
    prob_grads = jnp.einsum(
        "pikgd,pjkd->pkgij",
        context_gradient_rows,
        projected_value_rows,
        preferred_element_type=jnp.float32,
    )
    row_dot = jnp.sum(attention * prob_grads, -1, keepdims=True)
    score_grads = (attention * (prob_grads - row_dot) * score_scale).astype(jnp.bfloat16)
    query_gradient = jnp.einsum(
        "pkgij,pjkd->pikgd",
        score_grads[:, :, :, :SUFFIX_TOKENS, :],
        projected_key_rows,
        preferred_element_type=jnp.float32,
    )
    key_gradient = jnp.einsum(
        "pkgij,pikgd->pjkd",
        score_grads[..., PLEN : PLEN + SUFFIX_TOKENS],
        query_matrix,
        preferred_element_type=jnp.float32,
    )
    value_gradient = jnp.einsum(
        "pkgij,pikgd->pjkd",
        attention_low[..., PLEN : PLEN + SUFFIX_TOKENS],
        context_gradient_rows,
        preferred_element_type=jnp.float32,
    )
    return (query_gradient, key_gradient, value_gradient)


def butterfly_sum(x, axis):
    size = lax.axis_size(axis)
    if size & (size - 1):
        return lax.psum(x, axis)
    step = 1
    while step < size:
        pairs = [(i, i ^ step) for i in range(size)]
        x = x + lax.ppermute(x, axis, pairs)
        step *= 2
    return x


def butterfly_gather(x, axis, dim):
    size = lax.axis_size(axis)
    if size & (size - 1):
        return lax.all_gather(x, axis, axis=dim, tiled=True)
    index = lax.axis_index(axis)
    step = 1
    while step < size:
        pairs = [(i, i ^ step) for i in range(size)]
        other = lax.ppermute(x, axis, pairs)
        low = (index & step) == 0
        x = jnp.where(
            low, jnp.concatenate([x, other], dim), jnp.concatenate([other, x], dim)
        )
        step *= 2
    return x


def on_device(
    embed_table,
    suffix_ids,
    context,
    prompt_len,
    norm_gain,
    w_query,
    key_projection_weight,
    value_projection_weight,
    ctx_grad,
):
    voc_rows = embed_table.shape[0]
    vocab_start = (lax.axis_index("tp") * lax.axis_size("pr") + lax.axis_index("pr")) * voc_rows
    picked = (
        suffix_ids[:, None] - vocab_start == jnp.arange(voc_rows, dtype=jnp.int32)[None, :]
    ).astype(jnp.bfloat16)
    lookup = jnp.dot(picked, embed_table, preferred_element_type=jnp.float32).astype(jnp.bfloat16)
    suffix_rows = butterfly_sum(butterfly_sum(lookup, "pr"), "tp")
    features = butterfly_gather(context, "tp", 2)
    prompts = features.shape[0]
    query_width = w_query.shape[1]
    key_width = key_projection_weight.shape[1]
    joined = jnp.concatenate([w_query, key_projection_weight, value_projection_weight], 1)
    whole = lax.all_gather(joined, "pr", axis=0, tiled=True)
    tokens = jnp.concatenate(
        [
            features[:, :PLEN],
            jnp.broadcast_to(suffix_rows[None], (prompts, SUFFIX_TOKENS, MODEL_WIDTH)),
            features[:, PLEN:],
        ],
        1,
    )
    normed = normalize(tokens, norm_gain)
    all_in = normed.reshape(prompts * SEQUENCE_TOKENS, MODEL_WIDTH)
    projected = jnp.dot(all_in, whole, preferred_element_type=jnp.float32).reshape(
        prompts, SEQUENCE_TOKENS, query_width + 2 * key_width
    )
    query_matrix = projected[:, PLEN:, :query_width]
    projected_key_rows = projected[:, :, query_width : query_width + key_width]
    projected_value_rows = projected[:, :, query_width + key_width :]
    query_heads = query_width // HEAD_SIZE
    key_heads = key_width // HEAD_SIZE
    query_group_width = query_heads // key_heads
    cosine_table, sine_lookup_table = rope_tables(SEQUENCE_TOKENS)
    query_matrix = apply_rotation(
        query_matrix.reshape(prompts, QUERY_ROW_COUNT, query_heads, HEAD_SIZE),
        cosine_table[PLEN:],
        sine_lookup_table[PLEN:],
        1.0,
    ).astype(jnp.bfloat16)
    query_matrix = query_matrix.reshape(
        prompts, QUERY_ROW_COUNT, key_heads, query_group_width, HEAD_SIZE
    )
    projected_key_rows = apply_rotation(
        projected_key_rows.reshape(prompts, SEQUENCE_TOKENS, key_heads, HEAD_SIZE),
        cosine_table,
        sine_lookup_table,
        1.0,
    ).astype(jnp.bfloat16)
    projected_value_rows = projected_value_rows.reshape(
        prompts, SEQUENCE_TOKENS, key_heads, HEAD_SIZE
    ).astype(jnp.bfloat16)
    context_gradient_rows = ctx_grad.reshape(
        prompts, QUERY_ROW_COUNT, key_heads, query_group_width, HEAD_SIZE
    )
    query_gradient, key_gradient, value_gradient = attention_grads(
        query_matrix, projected_key_rows, projected_value_rows, context_gradient_rows, prompt_len
    )
    suffix_cos = cosine_table[PLEN : PLEN + SUFFIX_TOKENS]
    suffix_sin = sine_lookup_table[PLEN : PLEN + SUFFIX_TOKENS]
    query_gradient = apply_rotation(
        query_gradient.reshape(prompts, SUFFIX_TOKENS, query_heads, HEAD_SIZE),
        suffix_cos,
        suffix_sin,
        -1.0,
    )
    key_gradient = apply_rotation(key_gradient, suffix_cos, suffix_sin, -1.0)
    local_sums = jnp.concatenate(
        [
            jnp.sum(query_gradient, 0).reshape(SUFFIX_TOKENS, query_width),
            jnp.sum(key_gradient, 0).reshape(SUFFIX_TOKENS, key_width),
            jnp.sum(value_gradient, 0).reshape(SUFFIX_TOKENS, key_width),
        ],
        1,
    )
    rounded = butterfly_sum(local_sums, "pr").astype(jnp.bfloat16)
    suffix_f = suffix_rows.astype(jnp.float32)
    inverse = lax.rsqrt(jnp.mean(suffix_f * suffix_f, -1, keepdims=True) + NORM_EPS)
    gain_f = norm_gain.astype(jnp.float32)
    partial = lax.dot_general(
        rounded, whole, (((1,), (1,)), ((), ())), preferred_element_type=jnp.float32
    )
    hidden_grad = butterfly_sum(partial, "tp")
    scaled = gain_f * hidden_grad
    projection = jnp.sum(scaled * suffix_f, -1, keepdims=True)
    input_grad = (scaled * inverse - suffix_f * projection * inverse**3 / MODEL_WIDTH).astype(
        jnp.bfloat16
    )
    token_scores = lax.dot_general(
        input_grad, embed_table, (((1,), (1,)), ((), ())), preferred_element_type=jnp.float32
    )
    square_sum = butterfly_sum(
        butterfly_sum(jnp.sum(token_scores * token_scores, -1, keepdims=True), "pr"), "tp"
    )
    return token_scores * lax.rsqrt(square_sum / VOCAB + VOCAB_EPS)


def solution(mesh):
    placed = (
        P(("tp", "pr"), None),
        P(),
        P("pr", None, "tp"),
        P("pr"),
        P(),
        P("pr", "tp"),
        P("pr", "tp"),
        P("pr", "tp"),
        P("pr", None, "tp"),
    )
    return jax.shard_map(
        on_device, mesh=mesh, in_specs=placed, out_specs=P(None, ("tp", "pr")), check_vma=False
    )
```

```python
import jax
import jax.numpy as jnp
from jax import lax
from jax.sharding import PartitionSpec as P

MODEL_WIDTH = 8192
HEAD_SIZE = 128
VOCAB = 128256
PLEN = 32
SUFFIX_TOKENS = 20
SEQUENCE_TOKENS = 64
QUERY_ROW_COUNT = 32


NORM_EPS = 1e-05
VOCAB_EPS = 1e-06
ROPE_BASE = 500000.0


def rope_tables(count):
    positions = jnp.arange(count).astype(jnp.float32)
    frequency = ROPE_BASE ** (-(jnp.arange(HEAD_SIZE // 2).astype(jnp.float32) * (2.0 / HEAD_SIZE)))
    angles = positions[:, None] * frequency[None, :]
    return (jnp.cos(angles), jnp.sin(angles))


def apply_rotation(tensor, cosine_table, sine_lookup_table, direction):
    half_width = tensor.shape[-1] // 2
    first_half = tensor[..., :half_width]
    second_half = tensor[..., half_width:]
    cos_wide = cosine_table[:, None, :]
    sin_wide = sine_lookup_table[:, None, :] * direction
    return jnp.concatenate(
        [
            first_half * cos_wide - second_half * sin_wide,
            second_half * cos_wide + first_half * sin_wide,
        ],
        -1,
    )


def normalize(tokens, norm_gain):
    tokens_f = tokens.astype(jnp.float32)
    inverse = lax.rsqrt(jnp.mean(tokens_f * tokens_f, -1, keepdims=True) + NORM_EPS)
    return (tokens_f * inverse * norm_gain.astype(jnp.float32)).astype(jnp.bfloat16)


def attention_grads(
    query_matrix, projected_key_rows, projected_value_rows, context_gradient_rows, lengths
):
    score_scale = HEAD_SIZE ** (-0.5)
    scores = (
        jnp.einsum(
            "pikgd,pjkd->pkgij",
            query_matrix,
            projected_key_rows,
            preferred_element_type=jnp.float32,
        )
        * score_scale
    )
    query_pos = PLEN + jnp.arange(QUERY_ROW_COUNT)
    key_pos = jnp.arange(SEQUENCE_TOKENS)
    causal = key_pos[None, :] <= query_pos[:, None]
    unpadded = key_pos[None, :] >= (PLEN - lengths)[:, None]
    visible = (causal[None, :, :] & unpadded[:, None, :])[:, None, None, :, :]
    scores = jnp.where(visible, scores, -1e30)
    row_max = jnp.max(scores, -1, keepdims=True)
    expanded = jnp.where(visible, jnp.exp(scores - row_max), 0.0)
    attention = expanded / jnp.sum(expanded, -1, keepdims=True)
    attention_low = attention.astype(jnp.bfloat16)
    prob_grads = jnp.einsum(
        "pikgd,pjkd->pkgij",
        context_gradient_rows,
        projected_value_rows,
        preferred_element_type=jnp.float32,
    )
    row_dot = jnp.sum(attention * prob_grads, -1, keepdims=True)
    score_grads = (attention * (prob_grads - row_dot) * score_scale).astype(jnp.bfloat16)
    query_gradient = jnp.einsum(
        "pkgij,pjkd->pikgd",
        score_grads[:, :, :, :SUFFIX_TOKENS, :],
        projected_key_rows,
        preferred_element_type=jnp.float32,
    )
    key_gradient = jnp.einsum(
        "pkgij,pikgd->pjkd",
        score_grads[..., PLEN : PLEN + SUFFIX_TOKENS],
        query_matrix,
        preferred_element_type=jnp.float32,
    )
    value_gradient = jnp.einsum(
        "pkgij,pikgd->pjkd",
        attention_low[..., PLEN : PLEN + SUFFIX_TOKENS],
        context_gradient_rows,
        preferred_element_type=jnp.float32,
    )
    return (query_gradient, key_gradient, value_gradient)


def butterfly_sum(x, axis, radix=2):
    size = lax.axis_size(axis)
    if size & (size - 1):
        return lax.psum(x, axis)
    index = lax.axis_index(axis)
    step = 1
    while step < size:
        if radix == 4 and step * 4 <= size:
            digit = (index // step) % 4
            got = [None] + [
                lax.ppermute(x, axis, [(i, i ^ (d * step)) for i in range(size)])
                for d in (1, 2, 3)
            ]
            members = []
            for k in range(4):
                value = x
                for d in (1, 2, 3):
                    value = jnp.where(digit ^ d == k, got[d], value)
                members.append(value)
            x = (members[0] + members[1]) + (members[2] + members[3])
            step *= 4
        else:
            pairs = [(i, i ^ step) for i in range(size)]
            x = x + lax.ppermute(x, axis, pairs)
            step *= 2
    return x


def butterfly_gather(x, axis, dim):
    size = lax.axis_size(axis)
    if size & (size - 1):
        return lax.all_gather(x, axis, axis=dim, tiled=True)
    index = lax.axis_index(axis)
    step = 1
    while step < size:
        pairs = [(i, i ^ step) for i in range(size)]
        other = lax.ppermute(x, axis, pairs)
        low = (index & step) == 0
        x = jnp.where(
            low, jnp.concatenate([x, other], dim), jnp.concatenate([other, x], dim)
        )
        step *= 2
    return x


def on_device(
    embed_table,
    suffix_ids,
    context,
    prompt_len,
    norm_gain,
    w_query,
    key_projection_weight,
    value_projection_weight,
    ctx_grad,
):
    voc_rows = embed_table.shape[0]
    vocab_start = (lax.axis_index("tp") * lax.axis_size("pr") + lax.axis_index("pr")) * voc_rows
    picked = (
        suffix_ids[:, None] - vocab_start == jnp.arange(voc_rows, dtype=jnp.int32)[None, :]
    ).astype(jnp.bfloat16)
    lookup = jnp.dot(picked, embed_table, preferred_element_type=jnp.float32).astype(jnp.bfloat16)
    suffix_rows = butterfly_sum(butterfly_sum(lookup, "pr"), "tp")
    features = butterfly_gather(context, "tp", 2)
    prompts = features.shape[0]
    query_width = w_query.shape[1]
    key_width = key_projection_weight.shape[1]
    joined = jnp.concatenate([w_query, key_projection_weight, value_projection_weight], 1)
    whole = lax.all_gather(joined, "pr", axis=0, tiled=True)
    tokens = jnp.concatenate(
        [
            features[:, :PLEN],
            jnp.broadcast_to(suffix_rows[None], (prompts, SUFFIX_TOKENS, MODEL_WIDTH)),
            features[:, PLEN:],
        ],
        1,
    )
    normed = normalize(tokens, norm_gain)
    all_in = normed.reshape(prompts * SEQUENCE_TOKENS, MODEL_WIDTH)
    projected = jnp.dot(all_in, whole, preferred_element_type=jnp.float32).reshape(
        prompts, SEQUENCE_TOKENS, query_width + 2 * key_width
    )
    query_matrix = projected[:, PLEN:, :query_width]
    projected_key_rows = projected[:, :, query_width : query_width + key_width]
    projected_value_rows = projected[:, :, query_width + key_width :]
    query_heads = query_width // HEAD_SIZE
    key_heads = key_width // HEAD_SIZE
    query_group_width = query_heads // key_heads
    cosine_table, sine_lookup_table = rope_tables(SEQUENCE_TOKENS)
    query_matrix = apply_rotation(
        query_matrix.reshape(prompts, QUERY_ROW_COUNT, query_heads, HEAD_SIZE),
        cosine_table[PLEN:],
        sine_lookup_table[PLEN:],
        1.0,
    ).astype(jnp.bfloat16)
    query_matrix = query_matrix.reshape(
        prompts, QUERY_ROW_COUNT, key_heads, query_group_width, HEAD_SIZE
    )
    projected_key_rows = apply_rotation(
        projected_key_rows.reshape(prompts, SEQUENCE_TOKENS, key_heads, HEAD_SIZE),
        cosine_table,
        sine_lookup_table,
        1.0,
    ).astype(jnp.bfloat16)
    projected_value_rows = projected_value_rows.reshape(
        prompts, SEQUENCE_TOKENS, key_heads, HEAD_SIZE
    ).astype(jnp.bfloat16)
    context_gradient_rows = ctx_grad.reshape(
        prompts, QUERY_ROW_COUNT, key_heads, query_group_width, HEAD_SIZE
    )
    query_gradient, key_gradient, value_gradient = attention_grads(
        query_matrix, projected_key_rows, projected_value_rows, context_gradient_rows, prompt_len
    )
    suffix_cos = cosine_table[PLEN : PLEN + SUFFIX_TOKENS]
    suffix_sin = sine_lookup_table[PLEN : PLEN + SUFFIX_TOKENS]
    query_gradient = apply_rotation(
        query_gradient.reshape(prompts, SUFFIX_TOKENS, query_heads, HEAD_SIZE),
        suffix_cos,
        suffix_sin,
        -1.0,
    )
    key_gradient = apply_rotation(key_gradient, suffix_cos, suffix_sin, -1.0)
    local_sums = jnp.concatenate(
        [
            jnp.sum(query_gradient, 0).reshape(SUFFIX_TOKENS, query_width),
            jnp.sum(key_gradient, 0).reshape(SUFFIX_TOKENS, key_width),
            jnp.sum(value_gradient, 0).reshape(SUFFIX_TOKENS, key_width),
        ],
        1,
    )
    rounded = butterfly_sum(local_sums, "pr", 4).astype(jnp.bfloat16)
    suffix_f = suffix_rows.astype(jnp.float32)
    inverse = lax.rsqrt(jnp.mean(suffix_f * suffix_f, -1, keepdims=True) + NORM_EPS)
    gain_f = norm_gain.astype(jnp.float32)
    partial = lax.dot_general(
        rounded, whole, (((1,), (1,)), ((), ())), preferred_element_type=jnp.float32
    )
    hidden_grad = butterfly_sum(partial, "tp")
    scaled = gain_f * hidden_grad
    projection = jnp.sum(scaled * suffix_f, -1, keepdims=True)
    input_grad = (scaled * inverse - suffix_f * projection * inverse**3 / MODEL_WIDTH).astype(
        jnp.bfloat16
    )
    token_scores = lax.dot_general(
        input_grad, embed_table, (((1,), (1,)), ((), ())), preferred_element_type=jnp.float32
    )
    square_sum = butterfly_sum(
        butterfly_sum(jnp.sum(token_scores * token_scores, -1, keepdims=True), "pr", 4), "tp", 4
    )
    return token_scores * lax.rsqrt(square_sum / VOCAB + VOCAB_EPS)


def solution(mesh):
    placed = (
        P(("tp", "pr"), None),
        P(),
        P("pr", None, "tp"),
        P("pr"),
        P(),
        P("pr", "tp"),
        P("pr", "tp"),
        P("pr", "tp"),
        P("pr", None, "tp"),
    )
    return jax.shard_map(
        on_device, mesh=mesh, in_specs=placed, out_specs=P(None, ("tp", "pr")), check_vma=False
    )
```

```python
import jax
import jax.numpy as jnp
from jax import lax
from jax.sharding import PartitionSpec as P

MODEL_WIDTH = 8192
HEAD_SIZE = 128
VOCAB = 128256
PLEN = 32
SUFFIX_TOKENS = 20
SEQUENCE_TOKENS = 64
QUERY_ROW_COUNT = 32


NORM_EPS = 1e-05
VOCAB_EPS = 1e-06
ROPE_BASE = 500000.0


def rope_tables(count):
    positions = jnp.arange(count).astype(jnp.float32)
    frequency = ROPE_BASE ** (-(jnp.arange(HEAD_SIZE // 2).astype(jnp.float32) * (2.0 / HEAD_SIZE)))
    angles = positions[:, None] * frequency[None, :]
    return (jnp.cos(angles), jnp.sin(angles))


def apply_rotation(tensor, cosine_table, sine_lookup_table, direction):
    half_width = tensor.shape[-1] // 2
    first_half = tensor[..., :half_width]
    second_half = tensor[..., half_width:]
    cos_wide = cosine_table[:, None, :]
    sin_wide = sine_lookup_table[:, None, :] * direction
    return jnp.concatenate(
        [
            first_half * cos_wide - second_half * sin_wide,
            second_half * cos_wide + first_half * sin_wide,
        ],
        -1,
    )


def normalize(tokens, norm_gain):
    tokens_f = tokens.astype(jnp.float32)
    inverse = lax.rsqrt(jnp.mean(tokens_f * tokens_f, -1, keepdims=True) + NORM_EPS)
    return (tokens_f * inverse * norm_gain.astype(jnp.float32)).astype(jnp.bfloat16)


def attention_grads(
    query_matrix, projected_key_rows, projected_value_rows, context_gradient_rows, lengths
):
    score_scale = HEAD_SIZE ** (-0.5)
    scores = (
        jnp.einsum(
            "pikgd,pjkd->pkgij",
            query_matrix,
            projected_key_rows,
            preferred_element_type=jnp.float32,
        )
        * score_scale
    )
    query_pos = PLEN + jnp.arange(QUERY_ROW_COUNT)
    key_pos = jnp.arange(SEQUENCE_TOKENS)
    causal = key_pos[None, :] <= query_pos[:, None]
    unpadded = key_pos[None, :] >= (PLEN - lengths)[:, None]
    visible = (causal[None, :, :] & unpadded[:, None, :])[:, None, None, :, :]
    scores = jnp.where(visible, scores, -1e30)
    row_max = jnp.max(scores, -1, keepdims=True)
    expanded = jnp.where(visible, jnp.exp(scores - row_max), 0.0)
    attention = expanded / jnp.sum(expanded, -1, keepdims=True)
    attention_low = attention.astype(jnp.bfloat16)
    prob_grads = jnp.einsum(
        "pikgd,pjkd->pkgij",
        context_gradient_rows,
        projected_value_rows,
        preferred_element_type=jnp.float32,
    )
    row_dot = jnp.sum(attention * prob_grads, -1, keepdims=True)
    score_grads = (attention * (prob_grads - row_dot) * score_scale).astype(jnp.bfloat16)
    query_gradient = jnp.einsum(
        "pkgij,pjkd->pikgd",
        score_grads[:, :, :, :SUFFIX_TOKENS, :],
        projected_key_rows,
        preferred_element_type=jnp.float32,
    )
    key_gradient = jnp.einsum(
        "pkgij,pikgd->pjkd",
        score_grads[..., PLEN : PLEN + SUFFIX_TOKENS],
        query_matrix,
        preferred_element_type=jnp.float32,
    )
    value_gradient = jnp.einsum(
        "pkgij,pikgd->pjkd",
        attention_low[..., PLEN : PLEN + SUFFIX_TOKENS],
        context_gradient_rows,
        preferred_element_type=jnp.float32,
    )
    return (query_gradient, key_gradient, value_gradient)


def butterfly_sum(x, axis, radix=2):
    size = lax.axis_size(axis)
    if size & (size - 1):
        return lax.psum(x, axis)
    index = lax.axis_index(axis)
    step = 1
    while step < size:
        if radix == 4 and step * 4 <= size:
            digit = (index // step) % 4
            got = [None] + [
                lax.ppermute(x, axis, [(i, i ^ (d * step)) for i in range(size)])
                for d in (1, 2, 3)
            ]
            members = []
            for k in range(4):
                value = x
                for d in (1, 2, 3):
                    value = jnp.where(digit ^ d == k, got[d], value)
                members.append(value)
            x = (members[0] + members[1]) + (members[2] + members[3])
            step *= 4
        else:
            pairs = [(i, i ^ step) for i in range(size)]
            x = x + lax.ppermute(x, axis, pairs)
            step *= 2
    return x


def butterfly_gather(x, axis, dim):
    size = lax.axis_size(axis)
    if size & (size - 1):
        return lax.all_gather(x, axis, axis=dim, tiled=True)
    index = lax.axis_index(axis)
    step = 1
    while step < size:
        pairs = [(i, i ^ step) for i in range(size)]
        other = lax.ppermute(x, axis, pairs)
        low = (index & step) == 0
        x = jnp.where(
            low, jnp.concatenate([x, other], dim), jnp.concatenate([other, x], dim)
        )
        step *= 2
    return x


def halving_sum(x, axis, dim):
    size = lax.axis_size(axis)
    if size & (size - 1) or x.shape[dim] % size:
        return butterfly_sum(x, axis)
    index = lax.axis_index(axis)
    steps = []
    step = 1
    while step < size:
        steps.append(step)
        step *= 2
    for step in steps:
        pairs = [(i, i ^ step) for i in range(size)]
        low = (index & step) == 0
        first, second = jnp.split(x, 2, dim)
        keep = jnp.where(low, first, second)
        give = jnp.where(low, second, first)
        x = keep + lax.ppermute(give, axis, pairs)
    for step in steps[::-1]:
        pairs = [(i, i ^ step) for i in range(size)]
        low = (index & step) == 0
        other = lax.ppermute(x, axis, pairs)
        x = jnp.where(low, jnp.concatenate([x, other], dim), jnp.concatenate([other, x], dim))
    return x


def on_device(
    embed_table,
    suffix_ids,
    context,
    prompt_len,
    norm_gain,
    w_query,
    key_projection_weight,
    value_projection_weight,
    ctx_grad,
):
    voc_rows = embed_table.shape[0]
    vocab_start = (lax.axis_index("tp") * lax.axis_size("pr") + lax.axis_index("pr")) * voc_rows
    picked = (
        suffix_ids[:, None] - vocab_start == jnp.arange(voc_rows, dtype=jnp.int32)[None, :]
    ).astype(jnp.bfloat16)
    lookup = jnp.dot(picked, embed_table, preferred_element_type=jnp.float32).astype(jnp.bfloat16)
    suffix_rows = butterfly_sum(butterfly_sum(lookup, "pr"), "tp")
    features = butterfly_gather(context, "tp", 2)
    prompts = features.shape[0]
    query_width = w_query.shape[1]
    key_width = key_projection_weight.shape[1]
    joined = jnp.concatenate([w_query, key_projection_weight, value_projection_weight], 1)
    whole = lax.all_gather(joined, "pr", axis=0, tiled=True)
    tokens = jnp.concatenate(
        [
            features[:, :PLEN],
            jnp.broadcast_to(suffix_rows[None], (prompts, SUFFIX_TOKENS, MODEL_WIDTH)),
            features[:, PLEN:],
        ],
        1,
    )
    normed = normalize(tokens, norm_gain)
    all_in = normed.reshape(prompts * SEQUENCE_TOKENS, MODEL_WIDTH)
    projected = jnp.dot(all_in, whole, preferred_element_type=jnp.float32).reshape(
        prompts, SEQUENCE_TOKENS, query_width + 2 * key_width
    )
    query_matrix = projected[:, PLEN:, :query_width]
    projected_key_rows = projected[:, :, query_width : query_width + key_width]
    projected_value_rows = projected[:, :, query_width + key_width :]
    query_heads = query_width // HEAD_SIZE
    key_heads = key_width // HEAD_SIZE
    query_group_width = query_heads // key_heads
    cosine_table, sine_lookup_table = rope_tables(SEQUENCE_TOKENS)
    query_matrix = apply_rotation(
        query_matrix.reshape(prompts, QUERY_ROW_COUNT, query_heads, HEAD_SIZE),
        cosine_table[PLEN:],
        sine_lookup_table[PLEN:],
        1.0,
    ).astype(jnp.bfloat16)
    query_matrix = query_matrix.reshape(
        prompts, QUERY_ROW_COUNT, key_heads, query_group_width, HEAD_SIZE
    )
    projected_key_rows = apply_rotation(
        projected_key_rows.reshape(prompts, SEQUENCE_TOKENS, key_heads, HEAD_SIZE),
        cosine_table,
        sine_lookup_table,
        1.0,
    ).astype(jnp.bfloat16)
    projected_value_rows = projected_value_rows.reshape(
        prompts, SEQUENCE_TOKENS, key_heads, HEAD_SIZE
    ).astype(jnp.bfloat16)
    context_gradient_rows = ctx_grad.reshape(
        prompts, QUERY_ROW_COUNT, key_heads, query_group_width, HEAD_SIZE
    )
    query_gradient, key_gradient, value_gradient = attention_grads(
        query_matrix, projected_key_rows, projected_value_rows, context_gradient_rows, prompt_len
    )
    suffix_cos = cosine_table[PLEN : PLEN + SUFFIX_TOKENS]
    suffix_sin = sine_lookup_table[PLEN : PLEN + SUFFIX_TOKENS]
    query_gradient = apply_rotation(
        query_gradient.reshape(prompts, SUFFIX_TOKENS, query_heads, HEAD_SIZE),
        suffix_cos,
        suffix_sin,
        -1.0,
    )
    key_gradient = apply_rotation(key_gradient, suffix_cos, suffix_sin, -1.0)
    local_sums = jnp.concatenate(
        [
            jnp.sum(query_gradient, 0).reshape(SUFFIX_TOKENS, query_width),
            jnp.sum(key_gradient, 0).reshape(SUFFIX_TOKENS, key_width),
            jnp.sum(value_gradient, 0).reshape(SUFFIX_TOKENS, key_width),
        ],
        1,
    )
    rounded = butterfly_sum(local_sums, "pr", 4).astype(jnp.bfloat16)
    suffix_f = suffix_rows.astype(jnp.float32)
    inverse = lax.rsqrt(jnp.mean(suffix_f * suffix_f, -1, keepdims=True) + NORM_EPS)
    gain_f = norm_gain.astype(jnp.float32)
    partial = lax.dot_general(
        rounded, whole, (((1,), (1,)), ((), ())), preferred_element_type=jnp.float32
    )
    hidden_grad = halving_sum(partial, "tp", 1)
    scaled = gain_f * hidden_grad
    projection = jnp.sum(scaled * suffix_f, -1, keepdims=True)
    input_grad = (scaled * inverse - suffix_f * projection * inverse**3 / MODEL_WIDTH).astype(
        jnp.bfloat16
    )
    token_scores = lax.dot_general(
        input_grad, embed_table, (((1,), (1,)), ((), ())), preferred_element_type=jnp.float32
    )
    square_sum = butterfly_sum(
        butterfly_sum(jnp.sum(token_scores * token_scores, -1, keepdims=True), "pr", 4), "tp", 4
    )
    return token_scores * lax.rsqrt(square_sum / VOCAB + VOCAB_EPS)


def solution(mesh):
    placed = (
        P(("tp", "pr"), None),
        P(),
        P("pr", None, "tp"),
        P("pr"),
        P(),
        P("pr", "tp"),
        P("pr", "tp"),
        P("pr", "tp"),
        P("pr", None, "tp"),
    )
    return jax.shard_map(
        on_device, mesh=mesh, in_specs=placed, out_specs=P(None, ("tp", "pr")), check_vma=False
    )
```

```python
import jax
import jax.numpy as jnp
from jax import lax
from jax.sharding import PartitionSpec as P

MODEL_WIDTH = 8192
HEAD_SIZE = 128
VOCAB = 128256
PLEN = 32
SUFFIX_TOKENS = 20
SEQUENCE_TOKENS = 64
QUERY_ROW_COUNT = 32


NORM_EPS = 1e-05
VOCAB_EPS = 1e-06
ROPE_BASE = 500000.0


def rope_tables(count):
    positions = jnp.arange(count).astype(jnp.float32)
    frequency = ROPE_BASE ** (-(jnp.arange(HEAD_SIZE // 2).astype(jnp.float32) * (2.0 / HEAD_SIZE)))
    angles = positions[:, None] * frequency[None, :]
    return (jnp.cos(angles), jnp.sin(angles))


def apply_rotation(tensor, cosine_table, sine_lookup_table, direction):
    half_width = tensor.shape[-1] // 2
    first_half = tensor[..., :half_width]
    second_half = tensor[..., half_width:]
    cos_wide = cosine_table[:, None, :]
    sin_wide = sine_lookup_table[:, None, :] * direction
    return jnp.concatenate(
        [
            first_half * cos_wide - second_half * sin_wide,
            second_half * cos_wide + first_half * sin_wide,
        ],
        -1,
    )


def normalize(tokens, norm_gain):
    tokens_f = tokens.astype(jnp.float32)
    inverse = lax.rsqrt(jnp.mean(tokens_f * tokens_f, -1, keepdims=True) + NORM_EPS)
    return (tokens_f * inverse * norm_gain.astype(jnp.float32)).astype(jnp.bfloat16)


def attention_grads(
    query_matrix, projected_key_rows, projected_value_rows, context_gradient_rows, lengths
):
    score_scale = HEAD_SIZE ** (-0.5)
    scores = (
        jnp.einsum(
            "pikgd,pjkd->pkgij",
            query_matrix,
            projected_key_rows,
            preferred_element_type=jnp.float32,
        )
        * score_scale
    )
    query_pos = PLEN + jnp.arange(QUERY_ROW_COUNT)
    key_pos = jnp.arange(SEQUENCE_TOKENS)
    causal = key_pos[None, :] <= query_pos[:, None]
    unpadded = key_pos[None, :] >= (PLEN - lengths)[:, None]
    visible = (causal[None, :, :] & unpadded[:, None, :])[:, None, None, :, :]
    scores = jnp.where(visible, scores, -1e30)
    row_max = jnp.max(scores, -1, keepdims=True)
    expanded = jnp.where(visible, jnp.exp(scores - row_max), 0.0)
    attention = expanded / jnp.sum(expanded, -1, keepdims=True)
    attention_low = attention.astype(jnp.bfloat16)
    prob_grads = jnp.einsum(
        "pikgd,pjkd->pkgij",
        context_gradient_rows,
        projected_value_rows,
        preferred_element_type=jnp.float32,
    )
    row_dot = jnp.sum(attention * prob_grads, -1, keepdims=True)
    score_grads = (attention * (prob_grads - row_dot) * score_scale).astype(jnp.bfloat16)
    query_gradient = jnp.einsum(
        "pkgij,pjkd->pikgd",
        score_grads[:, :, :, :SUFFIX_TOKENS, :],
        projected_key_rows,
        preferred_element_type=jnp.float32,
    )
    key_gradient = jnp.einsum(
        "pkgij,pikgd->pjkd",
        score_grads[..., PLEN : PLEN + SUFFIX_TOKENS],
        query_matrix,
        preferred_element_type=jnp.float32,
    )
    value_gradient = jnp.einsum(
        "pkgij,pikgd->pjkd",
        attention_low[..., PLEN : PLEN + SUFFIX_TOKENS],
        context_gradient_rows,
        preferred_element_type=jnp.float32,
    )
    return (query_gradient, key_gradient, value_gradient)


def butterfly_sum(x, axis, radix=2):
    size = lax.axis_size(axis)
    if size & (size - 1):
        return lax.psum(x, axis)
    index = lax.axis_index(axis)
    step = 1
    while step < size:
        if radix == 4 and step * 4 <= size:
            digit = (index // step) % 4
            got = [None] + [
                lax.ppermute(x, axis, [(i, i ^ (d * step)) for i in range(size)])
                for d in (1, 2, 3)
            ]
            members = []
            for k in range(4):
                value = x
                for d in (1, 2, 3):
                    value = jnp.where(digit ^ d == k, got[d], value)
                members.append(value)
            x = (members[0] + members[1]) + (members[2] + members[3])
            step *= 4
        else:
            pairs = [(i, i ^ step) for i in range(size)]
            x = x + lax.ppermute(x, axis, pairs)
            step *= 2
    return x


def butterfly_gather(x, axis, dim):
    size = lax.axis_size(axis)
    if size & (size - 1):
        return lax.all_gather(x, axis, axis=dim, tiled=True)
    index = lax.axis_index(axis)
    step = 1
    while step < size:
        pairs = [(i, i ^ step) for i in range(size)]
        other = lax.ppermute(x, axis, pairs)
        low = (index & step) == 0
        x = jnp.where(
            low, jnp.concatenate([x, other], dim), jnp.concatenate([other, x], dim)
        )
        step *= 2
    return x


def halving_sum(x, axis, dim):
    size = lax.axis_size(axis)
    if size & (size - 1) or x.shape[dim] % size:
        return butterfly_sum(x, axis)
    index = lax.axis_index(axis)
    steps = []
    step = 1
    while step < size:
        steps.append(step)
        step *= 2
    for step in steps:
        pairs = [(i, i ^ step) for i in range(size)]
        low = (index & step) == 0
        first, second = jnp.split(x, 2, dim)
        keep = jnp.where(low, first, second)
        give = jnp.where(low, second, first)
        x = keep + lax.ppermute(give, axis, pairs)
    for step in steps[::-1]:
        pairs = [(i, i ^ step) for i in range(size)]
        low = (index & step) == 0
        other = lax.ppermute(x, axis, pairs)
        x = jnp.where(low, jnp.concatenate([x, other], dim), jnp.concatenate([other, x], dim))
    return x


def on_device(
    embed_table,
    suffix_ids,
    context,
    prompt_len,
    norm_gain,
    w_query,
    key_projection_weight,
    value_projection_weight,
    ctx_grad,
):
    voc_rows = embed_table.shape[0]
    vocab_start = (lax.axis_index("tp") * lax.axis_size("pr") + lax.axis_index("pr")) * voc_rows
    picked = (
        suffix_ids[:, None] - vocab_start == jnp.arange(voc_rows, dtype=jnp.int32)[None, :]
    ).astype(jnp.bfloat16)
    lookup = jnp.dot(picked, embed_table, preferred_element_type=jnp.float32).astype(jnp.bfloat16)
    suffix_rows = butterfly_sum(butterfly_sum(lookup, "pr"), "tp")
    features = butterfly_gather(context, "tp", 2)
    prompts = features.shape[0]
    query_width = w_query.shape[1]
    key_width = key_projection_weight.shape[1]
    joined = jnp.concatenate([w_query, key_projection_weight, value_projection_weight], 1)
    whole = lax.all_gather(joined, "pr", axis=0, tiled=True)
    tokens = jnp.concatenate(
        [
            features[:, :PLEN],
            jnp.broadcast_to(suffix_rows[None], (prompts, SUFFIX_TOKENS, MODEL_WIDTH)),
            features[:, PLEN:],
        ],
        1,
    )
    normed = normalize(tokens, norm_gain)
    all_in = normed.reshape(prompts * SEQUENCE_TOKENS, MODEL_WIDTH)
    projected = jnp.dot(all_in, whole, preferred_element_type=jnp.float32).reshape(
        prompts, SEQUENCE_TOKENS, query_width + 2 * key_width
    )
    query_matrix = projected[:, PLEN:, :query_width]
    projected_key_rows = projected[:, :, query_width : query_width + key_width]
    projected_value_rows = projected[:, :, query_width + key_width :]
    query_heads = query_width // HEAD_SIZE
    key_heads = key_width // HEAD_SIZE
    query_group_width = query_heads // key_heads
    cosine_table, sine_lookup_table = rope_tables(SEQUENCE_TOKENS)
    query_matrix = apply_rotation(
        query_matrix.reshape(prompts, QUERY_ROW_COUNT, query_heads, HEAD_SIZE),
        cosine_table[PLEN:],
        sine_lookup_table[PLEN:],
        1.0,
    ).astype(jnp.bfloat16)
    query_matrix = query_matrix.reshape(
        prompts, QUERY_ROW_COUNT, key_heads, query_group_width, HEAD_SIZE
    )
    projected_key_rows = apply_rotation(
        projected_key_rows.reshape(prompts, SEQUENCE_TOKENS, key_heads, HEAD_SIZE),
        cosine_table,
        sine_lookup_table,
        1.0,
    ).astype(jnp.bfloat16)
    projected_value_rows = projected_value_rows.reshape(
        prompts, SEQUENCE_TOKENS, key_heads, HEAD_SIZE
    ).astype(jnp.bfloat16)
    context_gradient_rows = ctx_grad.reshape(
        prompts, QUERY_ROW_COUNT, key_heads, query_group_width, HEAD_SIZE
    )
    query_gradient, key_gradient, value_gradient = attention_grads(
        query_matrix, projected_key_rows, projected_value_rows, context_gradient_rows, prompt_len
    )
    suffix_cos = cosine_table[PLEN : PLEN + SUFFIX_TOKENS]
    suffix_sin = sine_lookup_table[PLEN : PLEN + SUFFIX_TOKENS]
    query_gradient = apply_rotation(
        query_gradient.reshape(prompts, SUFFIX_TOKENS, query_heads, HEAD_SIZE),
        suffix_cos,
        suffix_sin,
        -1.0,
    )
    key_gradient = apply_rotation(key_gradient, suffix_cos, suffix_sin, -1.0)
    local_sums = jnp.concatenate(
        [
            jnp.sum(query_gradient, 0).reshape(SUFFIX_TOKENS, query_width),
            jnp.sum(key_gradient, 0).reshape(SUFFIX_TOKENS, key_width),
            jnp.sum(value_gradient, 0).reshape(SUFFIX_TOKENS, key_width),
        ],
        1,
    )
    rounded = butterfly_sum(local_sums, "pr", 4).astype(jnp.bfloat16)
    suffix_f = suffix_rows.astype(jnp.float32)
    inverse = lax.rsqrt(jnp.mean(suffix_f * suffix_f, -1, keepdims=True) + NORM_EPS)
    gain_f = norm_gain.astype(jnp.float32)
    half = whole.shape[0] // 2
    hidden_grad = jnp.concatenate(
        [
            halving_sum(
                lax.dot_general(
                    rounded, part, (((1,), (1,)), ((), ())), preferred_element_type=jnp.float32
                ),
                "tp",
                1,
            )
            for part in (whole[:half], whole[half:])
        ],
        1,
    )
    scaled = gain_f * hidden_grad
    projection = jnp.sum(scaled * suffix_f, -1, keepdims=True)
    input_grad = (scaled * inverse - suffix_f * projection * inverse**3 / MODEL_WIDTH).astype(
        jnp.bfloat16
    )
    token_scores = lax.dot_general(
        input_grad, embed_table, (((1,), (1,)), ((), ())), preferred_element_type=jnp.float32
    )
    square_sum = butterfly_sum(
        butterfly_sum(jnp.sum(token_scores * token_scores, -1, keepdims=True), "pr", 4), "tp", 4
    )
    return token_scores * lax.rsqrt(square_sum / VOCAB + VOCAB_EPS)


def solution(mesh):
    placed = (
        P(("tp", "pr"), None),
        P(),
        P("pr", None, "tp"),
        P("pr"),
        P(),
        P("pr", "tp"),
        P("pr", "tp"),
        P("pr", "tp"),
        P("pr", None, "tp"),
    )
    return jax.shard_map(
        on_device, mesh=mesh, in_specs=placed, out_specs=P(None, ("tp", "pr")), check_vma=False
    )
```
